512 devices in a mesh: dp: 8 (over y), cls: 64 (over x, z, core).
Axes of the slice: x: 4, y: 8, z: 8, core: 2. Of those that a mesh axis runs over, the one named last changes fastest.
Arguments:
- embeddings: bfloat16 [4608, 4096], P('dp'), may hold values from -128 to 128
- fold_ids: int32 [4608], P('dp'), may hold values from 0 to 4
- labels: int32 [4608], P('dp'), may hold values from 0 to 1023
- weights: bfloat16 [4096, 5120], P('dp', 'cls'), may hold values from -4 to 4
- direction: bfloat16 [4096, 5120], P('dp', 'cls'), may hold values from -0.09375 to 0.09375
Outputs:
- gradient: float32 [4096, 5120], P('dp', 'cls')
- hess_vec: float32 [4096, 5120], P('dp', 'cls')
The draws below stay inside these ranges and needn't reach their ends.
All inputs are finite; a program needn't handle non-finite values.
Results may differ from the reference program's by a relative error of at most 0.0055.
Values may be sent and summed in bfloat16 or wider, within the bound.
No kernel may reach another device: no remote copies, remote signals or barrier semaphores. Data moves between devices by JAX's collectives and lax.ppermute only.
A program may use at most 64 MiB of HBM per device.

```python
import math
import jax
import jax.numpy as jnp
from jax import lax

D = 4096
CLASSES = 1024
FOLDS = 5
ROWS = 4608
COLS = 5120


def weight_table(key):
    noise = jax.random.normal(jax.random.fold_in(key, 11), (D, COLS), jnp.float32)
    table = jnp.clip(noise, -6.0, 6.0) * (3.0 / math.sqrt(D))
    return table


def draw_weights(key, part):
    return weight_table(key).astype(jnp.bfloat16)


def draw_embeddings(key, part):
    base = jnp.clip(jax.random.normal(jax.random.fold_in(key, 23), (ROWS, D), jnp.float32), -6.0, 6.0)
    spread = jax.random.uniform(jax.random.fold_in(key, 24), (ROWS, 1), jnp.float32, math.log(0.4), math.log(4.0))
    values = base * jnp.exp(spread)
    return jnp.clip(values, -128.0, 128.0).astype(jnp.bfloat16)


def place_ends(values, own_key, low, high):
    longest = values.shape.index(max(values.shape))
    spots = []
    for shift in (0, 1):
        where = [jax.random.randint(jax.random.fold_in(own_key, axis), (), 0, length) for axis, length in enumerate(values.shape)]
        where[longest] = (where[longest] + shift) % values.shape[longest]
        spots.append(tuple(where))
    return values.at[spots[0]].set(low).at[spots[1]].set(high)


def shard_levels(rng, dims, split, smallest, top_value):
    level = 1.0
    for axis_at, parts in split:
        heights = jax.random.uniform(jax.random.fold_in(jax.random.fold_in(rng, 6), axis_at), (parts,), jnp.float32, smallest / len(split), top_value / len(split))
        level = level * jnp.repeat(jnp.exp(heights), dims[axis_at] // parts).reshape((-1,) + (1,) * (len(dims) - 1 - axis_at))
    return level


def centred(stream_key, dims, scale, limit, pieces=(), held_as=jnp.bfloat16):
    values = scale * jax.random.normal(stream_key, dims, jnp.float32)
    if pieces:
        values = values * shard_levels(stream_key, dims, pieces, -0.22, 0.18)
    return jnp.clip(values, -limit, limit).astype(held_as)


def setup_inputs(seed: int = 0) -> dict:
    key_list = jax.random.split(jax.random.key(seed), 6)
    return {
        "embeddings": draw_embeddings(jax.random.fold_in(key_list[5], 71), 0),
        "fold_ids": place_ends(jax.random.randint(key_list[1], (ROWS,), 0, FOLDS), jax.random.fold_in(key_list[1], 1), 0, FOLDS - 1).astype(jnp.int32),
        "labels": place_ends(jax.random.randint(key_list[2], (ROWS,), 0, CLASSES), jax.random.fold_in(key_list[2], 1), 0, CLASSES - 1).astype(jnp.int32),
        "weights": draw_weights(jax.random.fold_in(key_list[5], 71), 0),
        "direction": centred(key_list[4], (D, COLS), D ** -0.5, 0.09375, ((0, 8), (1, 64))),
    }


def reference(embeddings, fold_ids, labels, weights, direction):
    logits = jnp.dot(embeddings, weights, preferred_element_type=jnp.float32).reshape(ROWS, CLASSES, FOLDS)
    tangent = jnp.dot(embeddings, direction, preferred_element_type=jnp.float32).reshape(ROWS, CLASSES, FOLDS)
    highest = jnp.max(logits, axis=1, keepdims=True)
    scaled = jnp.exp(logits - highest)
    summed = jnp.sum(scaled, axis=1, keepdims=True)
    moment = jnp.sum(scaled * tangent, axis=1, keepdims=True)
    probability = scaled / summed
    mean_tangent = moment / summed
    onehot = (labels[:, None] == jnp.arange(CLASSES, dtype=jnp.int32)[None, :]).astype(jnp.float32)[:, :, None]
    training = (fold_ids[:, None] != jnp.arange(FOLDS, dtype=jnp.int32)[None, :]).astype(jnp.float32)[:, None, :]
    residual_rows = (training * (probability - onehot)).reshape(ROWS, COLS).astype(jnp.bfloat16)
    curvature = (training * probability * (tangent - mean_tangent)).reshape(ROWS, COLS).astype(jnp.bfloat16)
    contract = (((0,), (0,)), ((), ()))
    gradient = lax.dot_general(embeddings, residual_rows, contract, preferred_element_type=jnp.float32)
    hess_vec = lax.dot_general(embeddings, curvature, contract, preferred_element_type=jnp.float32)
    return gradient, hess_vec
```

```python
import jax
import jax.numpy as jnp
from jax import lax
from jax.sharding import PartitionSpec as P

FOLDS = 5
GATHER = "pp"


def gather_rows(x, axis, n):
    if GATHER == "ag":
        return lax.all_gather(x, axis, axis=0, tiled=True)
    me = lax.axis_index(axis)
    if GATHER == "dbl":
        held = x
        k = 0
        while (1 << k) < n:
            bit = 1 << k
            got = lax.ppermute(held, axis, [(i, i ^ bit) for i in range(n)])
            mine_low = (me & bit) == 0
            held = jnp.where(mine_low, jnp.concatenate([held, got], 0), jnp.concatenate([got, held], 0))
            k += 1
        return held
    parts = [x] + [lax.ppermute(x, axis, [(i, (i + k) % n) for i in range(n)]) for k in range(1, n)]
    reversed_parts = parts[::-1]
    doubled = jnp.concatenate(reversed_parts + reversed_parts, 0)
    start = ((n - 1 - me) % n) * x.shape[0]
    return lax.dynamic_slice_in_dim(doubled, start, n * x.shape[0], 0)


def softmax_stats(stats, axis, n):
    folds = stats.shape[1] // 3
    k = 0
    while (1 << k) < n:
        bit = 1 << k
        other = lax.ppermute(stats, axis, [(i, i ^ bit) for i in range(n)])
        m, mo = stats[:, :folds], other[:, :folds]
        top = jnp.maximum(m, mo)
        a = jnp.exp(m - top)
        b = jnp.exp(mo - top)
        a2 = jnp.concatenate([a, a], 1)
        b2 = jnp.concatenate([b, b], 1)
        rest = stats[:, folds:] * a2 + other[:, folds:] * b2
        stats = jnp.concatenate([top, rest], 1)
        k += 1
    return stats


def local(embeddings, fold_ids, labels, weights, direction):
    row_count = embeddings.shape[0]
    columns = weights.shape[1]
    per_class = columns // FOLDS
    n_dp = lax.axis_size("dp")
    n_cls = lax.axis_size("cls")
    both = gather_rows(jnp.concatenate([weights, direction], 1), "dp", n_dp)
    lt = jnp.dot(embeddings, both, preferred_element_type=jnp.float32)
    logits = lt[:, :columns].reshape(row_count, per_class, FOLDS)
    tangent = lt[:, columns:].reshape(row_count, per_class, FOLDS)
    local_high = jnp.max(logits, axis=1)
    scaled_local = jnp.exp(logits - local_high[:, None, :])
    stats = jnp.concatenate(
        [local_high, jnp.sum(scaled_local, axis=1), jnp.sum(scaled_local * tangent, axis=1)], 1
    )
    stats = softmax_stats(stats, "cls", n_cls)
    highest = stats[:, :FOLDS]
    summed = stats[:, FOLDS : 2 * FOLDS]
    moment = stats[:, 2 * FOLDS :]
    scaled = jnp.exp(logits - highest[:, None, :])
    probability = scaled / summed[:, None, :]
    mean_tangent = moment / summed
    class_ids = lax.axis_index("cls") * per_class + jnp.arange(per_class, dtype=jnp.int32)
    onehot = (labels[:, None] == class_ids[None, :]).astype(jnp.float32)[:, :, None]
    training = (fold_ids[:, None] != jnp.arange(FOLDS, dtype=jnp.int32)[None, :]).astype(
        jnp.float32
    )[:, None, :]
    residual_rows = (
        (training * (probability - onehot)).reshape(row_count, columns).astype(jnp.bfloat16)
    )
    curvature = (
        (training * probability * (tangent - mean_tangent[:, None, :]))
        .reshape(row_count, columns)
        .astype(jnp.bfloat16)
    )
    contract = (((0,), (0,)), ((), ()))
    terms = lax.dot_general(
        embeddings,
        jnp.concatenate([residual_rows, curvature], 1),
        contract,
        preferred_element_type=jnp.float32,
    )
    summed_terms = lax.psum_scatter(terms, "dp", scatter_dimension=0, tiled=True)
    return (summed_terms[:, :columns], summed_terms[:, columns:])


def solution(mesh):
    placed = (P("dp", None), P("dp"), P("dp"), P("dp", "cls"), P("dp", "cls"))
    return jax.shard_map(
        local,
        mesh=mesh,
        in_specs=placed,
        out_specs=(P("dp", "cls"), P("dp", "cls")),
        check_vma=False,
    )
```

```python
import jax
import jax.numpy as jnp
from jax import lax
from jax.sharding import Mesh, PartitionSpec as P

FOLDS = 5
CLS = ("x", "z", "c")
GATHER = "ag"
STATS = "ag2"


def gather_rows(x, axis, n):
    if GATHER == "ag":
        return lax.all_gather(x, axis, axis=0, tiled=True)
    me = lax.axis_index(axis)
    if GATHER == "dbl":
        held = x
        k = 0
        while (1 << k) < n:
            bit = 1 << k
            got = lax.ppermute(held, axis, [(i, i ^ bit) for i in range(n)])
            mine_low = (me & bit) == 0
            held = jnp.where(mine_low, jnp.concatenate([held, got], 0), jnp.concatenate([got, held], 0))
            k += 1
        return held
    parts = [x] + [lax.ppermute(x, axis, [(i, (i + k) % n) for i in range(n)]) for k in range(1, n)]
    reversed_parts = parts[::-1]
    doubled = jnp.concatenate(reversed_parts + reversed_parts, 0)
    start = ((n - 1 - me) % n) * x.shape[0]
    return lax.dynamic_slice_in_dim(doubled, start, n * x.shape[0], 0)


def softmax_stats(stats, axis, n):
    folds = stats.shape[1] // 3
    k = 0
    while (1 << k) < n:
        bit = 1 << k
        other = lax.ppermute(stats, axis, [(i, i ^ bit) for i in range(n)])
        m, mo = stats[:, :folds], other[:, :folds]
        top = jnp.maximum(m, mo)
        a = jnp.exp(m - top)
        b = jnp.exp(mo - top)
        a2 = jnp.concatenate([a, a], 1)
        b2 = jnp.concatenate([b, b], 1)
        rest = stats[:, folds:] * a2 + other[:, folds:] * b2
        stats = jnp.concatenate([top, rest], 1)
        k += 1
    return stats


def combine_many(gathered):
    folds = gathered.shape[2] // 3
    m = gathered[:, :, :folds]
    top = jnp.max(m, axis=0)
    scale = jnp.exp(m - top[None])
    summed = jnp.sum(gathered[:, :, folds : 2 * folds] * scale, axis=0)
    moment = jnp.sum(gathered[:, :, 2 * folds :] * scale, axis=0)
    return jnp.concatenate([top, summed, moment], 1)


def local(embeddings, fold_ids, labels, weights, direction):
    row_count = embeddings.shape[0]
    columns = weights.shape[1]
    per_class = columns // FOLDS
    n_dp = lax.axis_size("dp")
    n_cls = lax.axis_size(CLS)
    both = gather_rows(jnp.concatenate([weights, direction], 1), "dp", n_dp)
    lt = jnp.dot(embeddings, both, preferred_element_type=jnp.float32)
    logits = lt[:, :columns].reshape(row_count, per_class, FOLDS)
    tangent = lt[:, columns:].reshape(row_count, per_class, FOLDS)
    local_high = jnp.max(logits, axis=1)
    scaled_local = jnp.exp(logits - local_high[:, None, :])
    stats = jnp.concatenate(
        [local_high, jnp.sum(scaled_local, axis=1), jnp.sum(scaled_local * tangent, axis=1)], 1
    )
    if STATS == "ag2":
        stats = combine_many(lax.all_gather(stats, ("z", "c"), axis=0, tiled=False))
        stats = combine_many(lax.all_gather(stats, "x", axis=0, tiled=False))
    else:
        stats = softmax_stats(stats, CLS, n_cls)
    highest = stats[:, :FOLDS]
    summed = stats[:, FOLDS : 2 * FOLDS]
    moment = stats[:, 2 * FOLDS :]
    scaled = jnp.exp(logits - highest[:, None, :])
    probability = scaled / summed[:, None, :]
    mean_tangent = moment / summed
    class_ids = lax.axis_index(CLS) * per_class + jnp.arange(per_class, dtype=jnp.int32)
    onehot = (labels[:, None] == class_ids[None, :]).astype(jnp.float32)[:, :, None]
    training = (fold_ids[:, None] != jnp.arange(FOLDS, dtype=jnp.int32)[None, :]).astype(
        jnp.float32
    )[:, None, :]
    residual_rows = (
        (training * (probability - onehot)).reshape(row_count, columns).astype(jnp.bfloat16)
    )
    curvature = (
        (training * probability * (tangent - mean_tangent[:, None, :]))
        .reshape(row_count, columns)
        .astype(jnp.bfloat16)
    )
    contract = (((0,), (0,)), ((), ()))
    terms = lax.dot_general(
        embeddings,
        jnp.concatenate([residual_rows, curvature], 1),
        contract,
        preferred_element_type=jnp.float32,
    )
    summed_terms = lax.psum_scatter(terms, "dp", scatter_dimension=0, tiled=True)
    return (summed_terms[:, :columns], summed_terms[:, columns:])


def split_mesh(mesh):
    row = mesh.devices[0]
    nx = len({d.coords[0] for d in row})
    nz = len({d.coords[2] for d in row})
    nc = len(row) // (nx * nz)
    return Mesh(mesh.devices.reshape(mesh.devices.shape[0], nx, nz, nc), ("dp",) + CLS)


def solution(mesh):
    placed = (P("dp", None), P("dp"), P("dp"), P("dp", CLS), P("dp", CLS))
    return jax.shard_map(
        local,
        mesh=split_mesh(mesh),
        in_specs=placed,
        out_specs=(P("dp", CLS), P("dp", CLS)),
        check_vma=False,
    )
```

```python
import jax
import jax.numpy as jnp
from jax import lax
from jax.sharding import Mesh, PartitionSpec as P

FOLDS = 5
CLS = ("x", "z", "c")
GATHER = "ag"
STATS = "ag2"


def gather_rows(x, axis, n):
    if GATHER == "ag":
        return lax.all_gather(x, axis, axis=0, tiled=True)
    me = lax.axis_index(axis)
    if GATHER == "dbl":
        held = x
        k = 0
        while (1 << k) < n:
            bit = 1 << k
            got = lax.ppermute(held, axis, [(i, i ^ bit) for i in range(n)])
            mine_low = (me & bit) == 0
            held = jnp.where(mine_low, jnp.concatenate([held, got], 0), jnp.concatenate([got, held], 0))
            k += 1
        return held
    parts = [x] + [lax.ppermute(x, axis, [(i, (i + k) % n) for i in range(n)]) for k in range(1, n)]
    reversed_parts = parts[::-1]
    doubled = jnp.concatenate(reversed_parts + reversed_parts, 0)
    start = ((n - 1 - me) % n) * x.shape[0]
    return lax.dynamic_slice_in_dim(doubled, start, n * x.shape[0], 0)


def softmax_stats(stats, axis, n):
    folds = stats.shape[1] // 3
    k = 0
    while (1 << k) < n:
        bit = 1 << k
        other = lax.ppermute(stats, axis, [(i, i ^ bit) for i in range(n)])
        m, mo = stats[:, :folds], other[:, :folds]
        top = jnp.maximum(m, mo)
        a = jnp.exp(m - top)
        b = jnp.exp(mo - top)
        a2 = jnp.concatenate([a, a], 1)
        b2 = jnp.concatenate([b, b], 1)
        rest = stats[:, folds:] * a2 + other[:, folds:] * b2
        stats = jnp.concatenate([top, rest], 1)
        k += 1
    return stats


def combine_many(gathered):
    folds = gathered.shape[2] // 3
    m = gathered[:, :, :folds]
    top = jnp.max(m, axis=0)
    scale = jnp.exp(m - top[None])
    summed = jnp.sum(gathered[:, :, folds : 2 * folds] * scale, axis=0)
    moment = jnp.sum(gathered[:, :, 2 * folds :] * scale, axis=0)
    return jnp.concatenate([top, summed, moment], 1)


def local(embeddings, fold_ids, labels, weights, direction):
    row_count = embeddings.shape[0]
    columns = weights.shape[1]
    per_class = columns // FOLDS
    n_dp = lax.axis_size("dp")
    n_cls = lax.axis_size(CLS)
    mine = jnp.concatenate([weights, direction], 1)
    share = mine.shape[0]
    me = lax.axis_index("dp")
    lt = None
    for k in range(n_dp):
        part = mine if k == 0 else lax.ppermute(mine, "dp", [(i, (i + k) % n_dp) for i in range(n_dp)])
        cols = lax.dynamic_slice_in_dim(embeddings, ((me - k) % n_dp) * share, share, 1)
        step = jnp.dot(cols, part, preferred_element_type=jnp.float32)
        lt = step if lt is None else lt + step
    logits = lt[:, :columns].reshape(row_count, per_class, FOLDS)
    tangent = lt[:, columns:].reshape(row_count, per_class, FOLDS)
    local_high = jnp.max(logits, axis=1)
    scaled_local = jnp.exp(logits - local_high[:, None, :])
    stats = jnp.concatenate(
        [local_high, jnp.sum(scaled_local, axis=1), jnp.sum(scaled_local * tangent, axis=1)], 1
    )
    if STATS == "ag2":
        stats = combine_many(lax.all_gather(stats, ("z", "c"), axis=0, tiled=False))
        stats = combine_many(lax.all_gather(stats, "x", axis=0, tiled=False))
    else:
        stats = softmax_stats(stats, CLS, n_cls)
    highest = stats[:, :FOLDS]
    summed = stats[:, FOLDS : 2 * FOLDS]
    moment = stats[:, 2 * FOLDS :]
    scaled = jnp.exp(logits - highest[:, None, :])
    probability = scaled / summed[:, None, :]
    mean_tangent = moment / summed
    class_ids = lax.axis_index(CLS) * per_class + jnp.arange(per_class, dtype=jnp.int32)
    onehot = (labels[:, None] == class_ids[None, :]).astype(jnp.float32)[:, :, None]
    training = (fold_ids[:, None] != jnp.arange(FOLDS, dtype=jnp.int32)[None, :]).astype(
        jnp.float32
    )[:, None, :]
    residual_rows = (
        (training * (probability - onehot)).reshape(row_count, columns).astype(jnp.bfloat16)
    )
    curvature = (
        (training * probability * (tangent - mean_tangent[:, None, :]))
        .reshape(row_count, columns)
        .astype(jnp.bfloat16)
    )
    contract = (((0,), (0,)), ((), ()))
    terms = lax.dot_general(
        embeddings,
        jnp.concatenate([residual_rows, curvature], 1),
        contract,
        preferred_element_type=jnp.float32,
    )
    summed_terms = lax.psum_scatter(terms, "dp", scatter_dimension=0, tiled=True)
    return (summed_terms[:, :columns], summed_terms[:, columns:])


def split_mesh(mesh):
    row = mesh.devices[0]
    nx = len({d.coords[0] for d in row})
    nz = len({d.coords[2] for d in row})
    nc = len(row) // (nx * nz)
    return Mesh(mesh.devices.reshape(mesh.devices.shape[0], nx, nz, nc), ("dp",) + CLS)


def solution(mesh):
    placed = (P("dp", None), P("dp"), P("dp"), P("dp", CLS), P("dp", CLS))
    return jax.shard_map(
        local,
        mesh=split_mesh(mesh),
        in_specs=placed,
        out_specs=(P("dp", CLS), P("dp", CLS)),
        check_vma=False,
    )
```

```python
import jax
import jax.numpy as jnp
from jax import lax
from jax.sharding import Mesh, PartitionSpec as P

FOLDS = 5
CLS = ("x", "z", "c")
GATHER = "ag"
STATS = "ag2"


def gather_rows(x, axis, n):
    if GATHER == "ag":
        return lax.all_gather(x, axis, axis=0, tiled=True)
    me = lax.axis_index(axis)
    if GATHER == "dbl":
        held = x
        k = 0
        while (1 << k) < n:
            bit = 1 << k
            got = lax.ppermute(held, axis, [(i, i ^ bit) for i in range(n)])
            mine_low = (me & bit) == 0
            held = jnp.where(mine_low, jnp.concatenate([held, got], 0), jnp.concatenate([got, held], 0))
            k += 1
        return held
    parts = [x] + [lax.ppermute(x, axis, [(i, (i + k) % n) for i in range(n)]) for k in range(1, n)]
    reversed_parts = parts[::-1]
    doubled = jnp.concatenate(reversed_parts + reversed_parts, 0)
    start = ((n - 1 - me) % n) * x.shape[0]
    return lax.dynamic_slice_in_dim(doubled, start, n * x.shape[0], 0)


def softmax_stats(stats, axis, n):
    folds = stats.shape[1] // 3
    k = 0
    while (1 << k) < n:
        bit = 1 << k
        other = lax.ppermute(stats, axis, [(i, i ^ bit) for i in range(n)])
        m, mo = stats[:, :folds], other[:, :folds]
        top = jnp.maximum(m, mo)
        a = jnp.exp(m - top)
        b = jnp.exp(mo - top)
        a2 = jnp.concatenate([a, a], 1)
        b2 = jnp.concatenate([b, b], 1)
        rest = stats[:, folds:] * a2 + other[:, folds:] * b2
        stats = jnp.concatenate([top, rest], 1)
        k += 1
    return stats


def combine_many(gathered):
    folds = gathered.shape[2] // 3
    m = gathered[:, :, :folds]
    top = jnp.max(m, axis=0)
    scale = jnp.exp(m - top[None])
    summed = jnp.sum(gathered[:, :, folds : 2 * folds] * scale, axis=0)
    moment = jnp.sum(gathered[:, :, 2 * folds :] * scale, axis=0)
    return jnp.concatenate([top, summed, moment], 1)


def local(embeddings, fold_ids, labels, weights, direction):
    row_count = embeddings.shape[0]
    columns = weights.shape[1]
    per_class = columns // FOLDS
    n_dp = lax.axis_size("dp")
    n_cls = lax.axis_size(CLS)
    mine = jnp.concatenate([weights, direction], 1)
    share = mine.shape[0]
    me = lax.axis_index("dp")
    lt = None
    for k in range(n_dp):
        part = mine if k == 0 else lax.ppermute(mine, "dp", [(i, (i + k) % n_dp) for i in range(n_dp)])
        cols = lax.dynamic_slice_in_dim(embeddings, ((me - k) % n_dp) * share, share, 1)
        step = jnp.dot(cols, part, preferred_element_type=jnp.float32)
        lt = step if lt is None else lt + step
    logits = lt[:, :columns].reshape(row_count, per_class, FOLDS)
    tangent = lt[:, columns:].reshape(row_count, per_class, FOLDS)
    local_high = jnp.max(logits, axis=1)
    scaled_local = jnp.exp(logits - local_high[:, None, :])
    stats = jnp.concatenate(
        [local_high, jnp.sum(scaled_local, axis=1), jnp.sum(scaled_local * tangent, axis=1)], 1
    )
    if STATS == "ag2":
        stats = combine_many(lax.all_gather(stats, ("z", "c"), axis=0, tiled=False))
        stats = combine_many(lax.all_gather(stats, "x", axis=0, tiled=False))
    else:
        stats = softmax_stats(stats, CLS, n_cls)
    highest = stats[:, :FOLDS]
    summed = stats[:, FOLDS : 2 * FOLDS]
    moment = stats[:, 2 * FOLDS :]
    scaled = jnp.exp(logits - highest[:, None, :])
    probability = scaled / summed[:, None, :]
    mean_tangent = moment / summed
    class_ids = lax.axis_index(CLS) * per_class + jnp.arange(per_class, dtype=jnp.int32)
    onehot = (labels[:, None] == class_ids[None, :]).astype(jnp.float32)[:, :, None]
    training = (fold_ids[:, None] != jnp.arange(FOLDS, dtype=jnp.int32)[None, :]).astype(
        jnp.float32
    )[:, None, :]
    residual_rows = (
        (training * (probability - onehot)).reshape(row_count, columns).astype(jnp.bfloat16)
    )
    curvature = (
        (training * probability * (tangent - mean_tangent[:, None, :]))
        .reshape(row_count, columns)
        .astype(jnp.bfloat16)
    )
    contract = (((0,), (0,)), ((), ()))
    both_terms = jnp.concatenate([residual_rows, curvature], 1)
    feature_share = embeddings.shape[1] // n_dp
    summed_terms = None
    for k in range(n_dp):
        rows = lax.dynamic_slice_in_dim(embeddings, ((me + k) % n_dp) * feature_share, feature_share, 1)
        block = lax.dot_general(rows, both_terms, contract, preferred_element_type=jnp.float32)
        if k:
            sent = lax.ppermute(block.astype(jnp.bfloat16), "dp", [(i, (i + k) % n_dp) for i in range(n_dp)])
            block = sent.astype(jnp.float32)
        summed_terms = block if summed_terms is None else summed_terms + block
    return (summed_terms[:, :columns], summed_terms[:, columns:])


def split_mesh(mesh):
    row = mesh.devices[0]
    nx = len({d.coords[0] for d in row})
    nz = len({d.coords[2] for d in row})
    nc = len(row) // (nx * nz)
    return Mesh(mesh.devices.reshape(mesh.devices.shape[0], nx, nz, nc), ("dp",) + CLS)


def solution(mesh):
    placed = (P("dp", None), P("dp"), P("dp"), P("dp", CLS), P("dp", CLS))
    return jax.shard_map(
        local,
        mesh=split_mesh(mesh),
        in_specs=placed,
        out_specs=(P("dp", CLS), P("dp", CLS)),
        check_vma=False,
    )
```
